256 devices in a mesh: seq: 64 (over y, z, core), pb: 4 (over x).
Axes of the slice: x: 4, y: 4, z: 8, core: 2. Of those that a mesh axis runs over, the one named last changes fastest.
Arguments:
- tokens: bfloat16 [16384, 2048], P('seq'), may hold values from -0.119628906 to 0.119628906
- w_query: bfloat16 [2048, 2048], P(None, 'pb')
- w_key: bfloat16 [2048, 2048], P(None, 'pb')
- w_value: bfloat16 [2048, 2048], P(None, 'pb'), may hold values from -0.125 to 0.125
- w_out: bfloat16 [2048, 2048], P('pb'), may hold values from -0.125 to 0.125
- gain_attn: float32 [2048], replicated, may hold values from 0.1 to 1.9
- gain_embed: float32 [2048], replicated, may hold values from 0.1 to 1.9
- queries: bfloat16 [256, 32, 2048], P(('seq', 'pb')), may hold values from -0.125 to 0.125
- query_lengths: int32 [256], P(('seq', 'pb')), may hold values from 8 to 32
- group_lengths: int32 [128], replicated, may hold values from 1 to 1024, 16384 in all
- teacher: float32 [256, 128], P(('seq', 'pb')), may hold values from -12 to 12
Outputs:
- embedded: bfloat16 [16384, 2048], P('seq')
- scores: float32 [256, 128], P(('seq', 'pb'))
- score_gradient: float32 [256, 128], P(('seq', 'pb'))
- distill_loss: float32 [], replicated
The draws below stay inside these ranges and needn't reach their ends.
Inputs may be any that keep to these rules, and one draw needn't show every extreme that they name: `group_lengths`: the groups cover the document in order: the lengths sum to 16384.
All inputs are finite; a program needn't handle non-finite values.
Results may differ from the reference program's by a relative error of at most 0.013.
Values may be sent and summed in bfloat16 or wider, within the bound.
No kernel may reach another device: no remote copies, remote signals or barrier semaphores. Data moves between devices by JAX's collectives and lax.ppermute only.
A program may use at most 128 MiB of HBM per device.

```python
import math
import jax
import jax.numpy as jnp
import numpy as np
from jax import lax

D = 2048
HEADS = 16
HD = 128
WIN = 2048
LQ = 32
TOK_DEV = 256
TOKENS = 16384
QUERY_COUNT = 256
NCH = 128


def projection_base(key, salt_value):
    return jax.random.normal(jax.random.fold_in(key, salt_value), (D, D), jnp.float32) * D ** (-0.5)


def draw_w_query(key, part):
    return projection_base(key, 101).astype(jnp.bfloat16)


def draw_w_key(key, part):
    drawn = projection_base(key, 202)
    return drawn.astype(jnp.bfloat16)


def set_ends(result, key, smallest, largest):
    index_at = [jax.random.randint(jax.random.fold_in(key, axis), (), 0, length) for axis, length in enumerate(result.shape)]
    main_axis = result.shape.index(max(result.shape))
    next_to = index_at[:main_axis] + [(index_at[main_axis] + 1) % result.shape[main_axis]] + index_at[main_axis + 1:]
    return result.at[tuple(index_at)].set(smallest).at[tuple(next_to)].set(largest)


def shard_levels(stream_key, dims, shards, low, high):
    level = 1.0
    for position, blocks in shards:
        steps = jax.random.uniform(jax.random.fold_in(jax.random.fold_in(stream_key, 6), position), (blocks,), jnp.float32, low / len(shards), high / len(shards))
        level = level * jnp.repeat(jnp.exp(steps), dims[position] // blocks).reshape((-1,) + (1,) * (len(dims) - 1 - position))
    return level


def length_profile(amount, total, reach, lean):
    loads = [(1 << 20) // math.isqrt(grade ** lean) + 1 for grade in range(2, amount + 1)]
    rest, counts = total - reach - (amount - 1), [1] * (amount - 1)
    while rest > 0:
        movable = [i for i in range(amount - 1) if counts[i] < reach]
        mass, left = sum([loads[i] for i in movable]), rest
        for i in movable:
            extra = min(reach - counts[i], max(1, left * loads[i] // mass), rest)
            counts[i] = counts[i] + extra
            rest = rest - extra
    return np.array([reach] + counts)


def ragged(key, amount, total, most, lean):
    if amount == 2:
        one = jax.random.randint(key, (), max(1, total - most), min(most, total - 1) + 1)
        return jnp.stack([one, total - one])
    sizes = jnp.asarray(length_profile(amount, total, most, lean), jnp.int32)
    couples = (amount - 1) // 2
    source_of, receiver = sizes[1:1 + 2 * couples:2], sizes[2:2 + 2 * couples:2]
    room = jnp.minimum(source_of - 1, most - receiver)
    moved = jax.random.randint(jax.random.fold_in(key, 1), (couples,), 0, 1 << 20) % (room + 1)
    sizes = sizes.at[1:1 + 2 * couples:2].set(source_of - moved).at[2:2 + 2 * couples:2].set(receiver + moved)
    return sizes[jax.random.permutation(jax.random.fold_in(key, 2), amount)]


def noise(stream_key, dims, width, reach, shards=(), kind=jnp.bfloat16):
    factor_of = shard_levels(stream_key, dims, shards, -0.22, 0.18) if shards else 1.0
    values = jax.random.normal(stream_key, dims, jnp.float32) * width * factor_of
    return jnp.minimum(jnp.maximum(values, -reach), reach).astype(kind)


def setup_inputs(seed: int = 0) -> dict:
    arg_keys = jax.random.split(jax.random.key(seed), 12)
    tokens = noise(arg_keys[0], (TOKENS, D), 0.02, 0.119628906, ((0, 64),))
    w_query = draw_w_query(jax.random.fold_in(arg_keys[11], 71), 0)
    w_key = draw_w_key(jax.random.fold_in(arg_keys[11], 71), 0)
    w_value = noise(arg_keys[3], (D, D), D ** -0.5, 0.125, ((1, 4),))
    w_out = noise(arg_keys[4], (D, D), D ** -0.5, 0.125, ((0, 4),))
    gain_attn = jnp.clip(1.0 + 0.18 * jax.random.normal(arg_keys[5], (D,), jnp.float32), 0.1, 1.9)
    gain_embed = jnp.clip(1.0 + 0.18 * jax.random.normal(arg_keys[6], (D,), jnp.float32), 0.1, 1.9)
    queries = noise(arg_keys[7], (QUERY_COUNT, LQ, D), D ** -0.5, 0.125, ((0, 256),))
    query_lengths = set_ends(jax.random.randint(arg_keys[8], (QUERY_COUNT,), LQ // 4, LQ + 1), jax.random.fold_in(arg_keys[8], 1), LQ // 4, LQ).astype(jnp.int32)
    group_lengths = ragged(arg_keys[9], NCH, TOKENS, 4 * TOK_DEV, 2).astype(jnp.int32)
    teacher = noise(arg_keys[10], (QUERY_COUNT, NCH), 3.0, 12.0, ((0, 256),), jnp.float32)
    return dict(tokens=tokens, w_query=w_query, w_key=w_key, w_value=w_value, w_out=w_out, gain_attn=gain_attn, gain_embed=gain_embed, queries=queries, query_lengths=query_lengths, group_lengths=group_lengths, teacher=teacher)


EPSILON = 1e-06
SOFTMAX_TEMP = 0.1

def rms_scale(values, gain):
    mean_sq = lax.optimization_barrier(jnp.mean(values * values, axis=-1, keepdims=True))
    return values * lax.rsqrt(mean_sq + EPSILON) * gain

def segmented_max(values, group_id):
    span_len = values.shape[-1]
    stride = 1
    while stride < span_len:
        filler = jnp.full(values.shape[:-1] + (stride,), -jnp.inf, values.dtype)
        shifted = jnp.concatenate([filler, values[..., :-stride]], axis=-1)
        prior_id = jnp.concatenate([jnp.full((stride,), -1, jnp.int32), group_id[:-stride]])
        values = jnp.where((prior_id == group_id)[None, :], jnp.maximum(values, shifted), values)
        stride = stride * 2
    return values

def reference(tokens, w_query, w_key, w_value, w_out, gain_attn, gain_embed, queries, query_lengths, group_lengths, teacher):
    half_win = WIN // 2
    residual = tokens.astype(jnp.float32)
    normed = rms_scale(residual, gain_attn).astype(jnp.bfloat16)
    q_all = jnp.dot(normed, w_query, preferred_element_type=jnp.float32).astype(jnp.bfloat16)
    k_all = jnp.dot(normed, w_key, preferred_element_type=jnp.float32).astype(jnp.bfloat16)
    v_all = jnp.dot(normed, w_value, preferred_element_type=jnp.float32).astype(jnp.bfloat16)
    k_pad = jnp.pad(k_all, ((half_win, half_win), (0, 0)))
    v_pad = jnp.pad(v_all, ((half_win, half_win), (0, 0)))
    block_rows = math.gcd(512, TOKENS)
    span_rows = block_rows + 2 * half_win

    def attend(block_index):
        first_row = (block_index * block_rows).astype(jnp.int32)
        q_block = lax.dynamic_slice_in_dim(q_all, first_row, block_rows, 0).reshape(block_rows, HEADS, HD).astype(jnp.float32)
        k_block = lax.dynamic_slice_in_dim(k_pad, first_row, span_rows, 0).reshape(span_rows, HEADS, HD).astype(jnp.float32)
        v_block = lax.dynamic_slice_in_dim(v_pad, first_row, span_rows, 0).reshape(span_rows, HEADS, HD).astype(jnp.float32)
        logits = jnp.einsum('qhd,khd->hqk', q_block, k_block) * HD ** (-0.5)
        q_pos = first_row + jnp.arange(block_rows, dtype=jnp.int32)
        k_pos = first_row - half_win + jnp.arange(span_rows, dtype=jnp.int32)
        in_window = (jnp.abs(q_pos[:, None] - k_pos[None, :]) <= half_win) & (k_pos >= 0)[None, :] & (k_pos < TOKENS)[None, :]
        logits = jnp.where(in_window[None], logits, -jnp.inf)
        row_max = lax.optimization_barrier(jnp.max(logits, axis=-1, keepdims=True))
        exp_terms = jnp.exp(logits - row_max)
        weights = (exp_terms / lax.optimization_barrier(jnp.sum(exp_terms, axis=-1, keepdims=True))).astype(jnp.bfloat16)
        mixed = jnp.einsum('hqk,khd->qhd', weights.astype(jnp.float32), v_block)
        return mixed.reshape(block_rows, HEADS * HD).astype(jnp.bfloat16)
    heads_out = lax.map(attend, jnp.arange(TOKENS // block_rows, dtype=jnp.int32)).reshape(TOKENS, HEADS * HD)
    attn_sum = jnp.dot(heads_out, w_out, preferred_element_type=jnp.float32)
    embedded = rms_scale(residual + attn_sum, gain_embed).astype(jnp.bfloat16)
    group_end = jnp.cumsum(group_lengths).astype(jnp.int32)
    positions = jnp.arange(TOKENS, dtype=jnp.int32)
    group_id = lax.optimization_barrier(jnp.sum((group_end[None, :] <= positions[:, None]).astype(jnp.int32), axis=1)).astype(jnp.int32)
    last_token = (group_end - 1).astype(jnp.int32)

    def score_one(query_item):
        q_tok, length = query_item
        similar = jnp.dot(q_tok, embedded.T, preferred_element_type=jnp.float32)
        running = segmented_max(similar, group_id)
        picked = jnp.take(running, last_token, axis=1)
        live_mask = (jnp.arange(LQ, dtype=jnp.int32) < length).astype(jnp.float32)
        return lax.optimization_barrier(jnp.sum(picked * live_mask[:, None], axis=0)) / length.astype(jnp.float32)
    scores = lax.map(score_one, (queries, query_lengths))
    student_scores = scores / SOFTMAX_TEMP
    student_scores = student_scores - lax.optimization_barrier(jnp.max(student_scores, axis=-1, keepdims=True))
    student_log_prob = student_scores - jnp.log(lax.optimization_barrier(jnp.sum(jnp.exp(student_scores), axis=-1, keepdims=True)))
    target_scores = teacher / SOFTMAX_TEMP
    target_scores = target_scores - lax.optimization_barrier(jnp.max(target_scores, axis=-1, keepdims=True))
    log_t = target_scores - jnp.log(lax.optimization_barrier(jnp.sum(jnp.exp(target_scores), axis=-1, keepdims=True)))
    teacher_prob = jnp.exp(log_t)
    kl_terms = lax.optimization_barrier(jnp.sum(teacher_prob * (log_t - student_log_prob), axis=-1))
    distill_loss = jnp.sum(kl_terms) / QUERY_COUNT
    score_gradient = (jnp.exp(student_log_prob) - teacher_prob) / (SOFTMAX_TEMP * QUERY_COUNT)
    return (embedded, scores, score_gradient, distill_loss)
```

```python
import jax
import jax.numpy as jnp
from jax import lax
from jax.sharding import PartitionSpec as P

HD = 128
WIN = 2048
LQ = 32


EPSILON = 1e-06
SOFTMAX_TEMP = 0.1


def shifted_2(x, axis, by):
    count = lax.axis_size(axis)
    pairs = [(i, i + by) for i in range(count) if 0 <= i + by < count]
    return lax.ppermute(x, axis, pairs)


def xor_swap(x, axis, bit):
    count = lax.axis_size(axis)
    return lax.ppermute(x, axis, [(i, i ^ bit) for i in range(count)])


def ring_shift(x, axis, by):
    count = lax.axis_size(axis)
    return lax.ppermute(x, axis, [(i, (i + by) % count) for i in range(count)])


HALVING_BITS = (1, 2, 16, 4, 32, 8)


def halving_max(values, axis):
    place = lax.axis_index(axis)
    rows = values.shape[0]
    width = rows.bit_length() - 1
    bits = [b for b in HALVING_BITS if b < rows]
    split = values.reshape((2,) * width + values.shape[1:])
    order = [width - 1 - (b.bit_length() - 1) for b in bits]
    split = jnp.transpose(split, order + list(range(width, split.ndim)))
    values = split.reshape((rows,) + values.shape[1:])
    for bit in bits:
        half = values.shape[0] // 2
        mine = ((place & bit) != 0).astype(jnp.int32)
        keep = lax.dynamic_slice_in_dim(values, mine * half, half, 0)
        send = lax.dynamic_slice_in_dim(values, (1 - mine) * half, half, 0)
        values = jnp.maximum(keep, xor_swap(send, axis, bit))
    return values


def butterfly_sum(value, axis):
    count = lax.axis_size(axis)
    bits = [b for b in HALVING_BITS if b < count]
    for bit in bits:
        value = value + xor_swap(value, axis, bit)
    return value


def rms_scale(values, gain):
    mean_sq = jnp.mean(values * values, axis=-1, keepdims=True)
    return values * lax.rsqrt(mean_sq + EPSILON) * gain


def segmented_max(values, group_id):
    span_len = values.shape[-1]
    stride = 1
    while stride < span_len:
        filler = jnp.full(values.shape[:-1] + (stride,), -jnp.inf, values.dtype)
        shifted = jnp.concatenate([filler, values[..., :-stride]], axis=-1)
        prior_id = jnp.concatenate([jnp.full((stride,), -1, jnp.int32), group_id[:-stride]])
        values = jnp.where((prior_id == group_id)[None, :], jnp.maximum(values, shifted), values)
        stride = stride * 2
    return values


def per_device(
    tokens,
    w_query,
    w_key,
    w_value,
    w_out,
    gain_attn,
    gain_embed,
    queries,
    query_lengths,
    group_lengths,
    teacher,
):
    shard_rows = tokens.shape[0]
    seq_count = lax.axis_size("seq")
    seq_place = lax.axis_index("seq")
    head_width = w_query.shape[1]
    heads_here = head_width // HD
    half_win = WIN // 2
    reach_count = half_win // shard_rows
    my_start = seq_place * shard_rows
    total_tokens = shard_rows * seq_count
    residual = tokens.astype(jnp.float32)
    normed = rms_scale(residual, gain_attn).astype(jnp.bfloat16)
    q_local = jnp.dot(normed, w_query, preferred_element_type=jnp.float32).astype(jnp.bfloat16)
    k_local = jnp.dot(normed, w_key, preferred_element_type=jnp.float32).astype(jnp.bfloat16)
    v_local = jnp.dot(normed, w_value, preferred_element_type=jnp.float32).astype(jnp.bfloat16)
    key_value = jnp.stack([k_local, v_local])
    earlier = [shifted_2(key_value, "seq", distance) for distance in range(reach_count, 0, -1)]
    later = [shifted_2(key_value, "seq", -distance) for distance in range(1, reach_count + 1)]
    window = jnp.concatenate(earlier + [key_value] + later, axis=1)
    span_rows = window.shape[1]
    q_pos = my_start + jnp.arange(shard_rows, dtype=jnp.int32)
    k_pos = my_start - reach_count * shard_rows + jnp.arange(span_rows, dtype=jnp.int32)
    in_window = (
        (jnp.abs(q_pos[:, None] - k_pos[None, :]) <= half_win)
        & (k_pos >= 0)[None, :]
        & (k_pos < total_tokens)[None, :]
    )
    q_heads = q_local.reshape(shard_rows, heads_here, HD)
    k_heads = window[0].reshape(span_rows, heads_here, HD)
    v_heads = window[1].reshape(span_rows, heads_here, HD)
    logits = jnp.einsum(
        "qhd,khd->hqk", q_heads, k_heads, preferred_element_type=jnp.float32
    ) * HD ** (-0.5)
    logits = jnp.where(in_window[None], logits, -jnp.inf)
    row_max = jnp.max(logits, axis=-1, keepdims=True)
    exp_terms = jnp.exp(logits - row_max)
    weights = (exp_terms / jnp.sum(exp_terms, axis=-1, keepdims=True)).astype(jnp.bfloat16)
    mixed = jnp.einsum("hqk,khd->qhd", weights, v_heads, preferred_element_type=jnp.float32)
    mixed = mixed.reshape(shard_rows, head_width).astype(jnp.bfloat16)
    pb_count = lax.axis_size("pb")
    mixed_parts = [mixed] + [ring_shift(mixed, "pb", k) for k in range(1, pb_count)]
    w_out_parts = [w_out] + [ring_shift(w_out, "pb", k) for k in range(1, pb_count)]
    attn_sum = jnp.dot(
        jnp.concatenate(mixed_parts, axis=1),
        jnp.concatenate(w_out_parts, axis=0),
        preferred_element_type=jnp.float32,
    )
    embedded = rms_scale(residual + attn_sum, gain_embed).astype(jnp.bfloat16)
    group_end = jnp.cumsum(group_lengths)
    group_start = group_end - group_lengths
    group_id = jnp.sum((group_end[None, :] <= q_pos[:, None]).astype(jnp.int32), axis=1)
    last_local = jnp.clip(group_end - 1 - my_start, 0, shard_rows - 1)
    present = (group_start < my_start + shard_rows) & (group_end > my_start)
    q_piece = lax.all_gather(queries, "seq", axis=0, tiled=True)
    count = q_piece.shape[0]
    q_rows = q_piece.reshape(count * q_piece.shape[1], q_piece.shape[2])
    similar = jnp.einsum("td,rd->tr", q_rows, embedded, preferred_element_type=jnp.float32)
    running = segmented_max(similar, group_id)
    picked = jnp.take(running, last_local, axis=1)
    picked = jnp.where(present[None, :], picked, -jnp.inf)
    part_max = picked.reshape(count, q_piece.shape[1], picked.shape[-1])
    own_count = queries.shape[0]
    token_max = halving_max(part_max, "seq")
    live_mask = (jnp.arange(LQ, dtype=jnp.int32)[None, :] < query_lengths[:, None]).astype(
        jnp.float32
    )
    scores = (
        jnp.sum(token_max * live_mask[:, :, None], axis=1)
        / query_lengths.astype(jnp.float32)[:, None]
    )
    student_scores = scores / SOFTMAX_TEMP
    student_scores = student_scores - jnp.max(student_scores, axis=-1, keepdims=True)
    student_log_prob = student_scores - jnp.log(
        jnp.sum(jnp.exp(student_scores), axis=-1, keepdims=True)
    )
    target_scores = teacher / SOFTMAX_TEMP
    target_scores = target_scores - jnp.max(target_scores, axis=-1, keepdims=True)
    log_t = target_scores - jnp.log(jnp.sum(jnp.exp(target_scores), axis=-1, keepdims=True))
    teacher_prob = jnp.exp(log_t)
    kl_terms = jnp.sum(teacher_prob * (log_t - student_log_prob), axis=-1)
    query_count_all = own_count * seq_count * lax.axis_size("pb")
    loss_sum = butterfly_sum(butterfly_sum(jnp.sum(kl_terms), "seq"), "pb")
    distill_loss = loss_sum / query_count_all
    score_gradient = (jnp.exp(student_log_prob) - teacher_prob) / (SOFTMAX_TEMP * query_count_all)
    return (embedded, scores, score_gradient, distill_loss)


def solution(mesh):
    placed = (
        P("seq", None),
        P(None, "pb"),
        P(None, "pb"),
        P(None, "pb"),
        P("pb", None),
        P(),
        P(),
        P(("seq", "pb"), None, None),
        P(("seq", "pb")),
        P(),
        P(("seq", "pb"), None),
    )
    return jax.shard_map(
        per_device,
        mesh=mesh,
        in_specs=placed,
        out_specs=(P("seq", None), P(("seq", "pb"), None), P(("seq", "pb"), None), P()),
        check_vma=False,
    )
```

```python
import jax
import jax.numpy as jnp
from jax import lax
from jax.sharding import PartitionSpec as P


HD = 128
WIN = 2048
LQ = 32


EPSILON = 1e-06
SOFTMAX_TEMP = 0.1


def sided_fetch(x, axis, distance):
    count = lax.axis_size(axis)
    pairs = []
    for target in range(count):
        source = target - distance if target % 2 == 0 else target + distance
        if 0 <= source < count:
            pairs.append((source, target))
    return lax.ppermute(x, axis, pairs)


def xor_swap(x, axis, bit):
    count = lax.axis_size(axis)
    return lax.ppermute(x, axis, [(i, i ^ bit) for i in range(count)])


def ring_shift(x, axis, by):
    count = lax.axis_size(axis)
    return lax.ppermute(x, axis, [(i, (i + by) % count) for i in range(count)])


HALVING_BITS = (1, 2, 16, 4, 32, 8)


def halving_max(values, axis):
    place = lax.axis_index(axis)
    rows = values.shape[0]
    width = rows.bit_length() - 1
    bits = [b for b in HALVING_BITS if b < rows]
    split = values.reshape((2,) * width + values.shape[1:])
    order = [width - 1 - (b.bit_length() - 1) for b in bits]
    split = jnp.transpose(split, order + list(range(width, split.ndim)))
    values = split.reshape((rows,) + values.shape[1:])
    for bit in bits:
        half = values.shape[0] // 2
        mine = ((place & bit) != 0).astype(jnp.int32)
        keep = lax.dynamic_slice_in_dim(values, mine * half, half, 0)
        send = lax.dynamic_slice_in_dim(values, (1 - mine) * half, half, 0)
        values = jnp.maximum(keep, xor_swap(send, axis, bit))
    return values


def butterfly_sum(value, axis):
    count = lax.axis_size(axis)
    bits = [b for b in HALVING_BITS if b < count]
    for bit in bits:
        value = value + xor_swap(value, axis, bit)
    return value


def rms_scale(values, gain):
    mean_sq = jnp.mean(values * values, axis=-1, keepdims=True)
    return values * lax.rsqrt(mean_sq + EPSILON) * gain


def segmented_max(values, group_id):
    span_len = values.shape[-1]
    stride = 1
    while stride < span_len:
        filler = jnp.full(values.shape[:-1] + (stride,), -jnp.inf, values.dtype)
        shifted = jnp.concatenate([filler, values[..., :-stride]], axis=-1)
        prior_id = jnp.concatenate([jnp.full((stride,), -1, jnp.int32), group_id[:-stride]])
        values = jnp.where((prior_id == group_id)[None, :], jnp.maximum(values, shifted), values)
        stride = stride * 2
    return values


def per_device(
    tokens,
    w_query,
    w_key,
    w_value,
    w_out,
    gain_attn,
    gain_embed,
    queries,
    query_lengths,
    group_lengths,
    teacher,
):
    shard_rows = tokens.shape[0]
    seq_count = lax.axis_size("seq")
    seq_place = lax.axis_index("seq")
    head_width = w_query.shape[1]
    heads_here = head_width // HD
    half_win = WIN // 2
    reach_count = half_win // shard_rows
    my_start = seq_place * shard_rows
    total_tokens = shard_rows * seq_count
    residual = tokens.astype(jnp.float32)
    normed = rms_scale(residual, gain_attn).astype(jnp.bfloat16)
    pb_count = lax.axis_size("pb")
    w_out_parts = [w_out] + [ring_shift(w_out, "pb", k) for k in range(1, pb_count)]
    q_local = jnp.dot(normed, w_query, preferred_element_type=jnp.float32).astype(jnp.bfloat16)
    k_local = jnp.dot(normed, w_key, preferred_element_type=jnp.float32).astype(jnp.bfloat16)
    v_local = jnp.dot(normed, w_value, preferred_element_type=jnp.float32).astype(jnp.bfloat16)
    core = seq_place % 2
    toward = 2 * core - 1
    k_heads_local = k_local.reshape(shard_rows, heads_here, HD).transpose(1, 0, 2)
    v_heads_local = v_local.reshape(shard_rows, heads_here, HD).transpose(1, 0, 2)
    key_value = jnp.stack([k_heads_local, v_heads_local])
    fetched = [sided_fetch(key_value, "seq", distance) for distance in range(1, reach_count + 1)]
    handed = lax.ppermute(
        jnp.stack([key_value] + fetched[: reach_count - 1]),
        "seq",
        [(i, i ^ 1) for i in range(seq_count)],
    )
    blocks = [key_value] + fetched + [handed[j] for j in range(reach_count)]
    window = jnp.concatenate(blocks, axis=2)
    span_rows = window.shape[2]
    block_shift = jnp.asarray(
        [0] + list(range(1, reach_count + 1)) + [-d for d in range(1, reach_count + 1)], jnp.int32
    )
    block_start = (seq_place + toward * block_shift) * shard_rows
    q_pos = my_start + jnp.arange(shard_rows, dtype=jnp.int32)
    k_pos = (block_start[:, None] + jnp.arange(shard_rows, dtype=jnp.int32)[None, :]).reshape(span_rows)
    in_window = (
        (jnp.abs(q_pos[:, None] - k_pos[None, :]) <= half_win)
        & (k_pos >= 0)[None, :]
        & (k_pos < total_tokens)[None, :]
    )
    q_heads = q_local.reshape(shard_rows, heads_here, HD).transpose(1, 0, 2)
    k_heads = window[0]
    v_heads = window[1]
    logits = jnp.einsum(
        "hqd,hkd->hqk", q_heads, k_heads, preferred_element_type=jnp.float32
    ) * HD ** (-0.5)
    logits = jnp.where(in_window[None], logits, -jnp.inf)
    row_max = jnp.max(logits, axis=-1, keepdims=True)
    exp_terms = jnp.exp(logits - row_max)
    weights = (exp_terms / jnp.sum(exp_terms, axis=-1, keepdims=True)).astype(jnp.bfloat16)
    mixed = jnp.einsum("hqk,hkd->qhd", weights, v_heads, preferred_element_type=jnp.float32)
    mixed = mixed.reshape(shard_rows, head_width).astype(jnp.bfloat16)
    mixed_parts = [mixed] + [ring_shift(mixed, "pb", k) for k in range(1, pb_count)]
    attn_sum = jnp.dot(
        jnp.concatenate(mixed_parts, axis=1),
        jnp.concatenate(w_out_parts, axis=0),
        preferred_element_type=jnp.float32,
    )
    embedded = rms_scale(residual + attn_sum, gain_embed).astype(jnp.bfloat16)
    group_end = jnp.cumsum(group_lengths)
    group_start = group_end - group_lengths
    group_id = jnp.sum((group_end[None, :] <= q_pos[:, None]).astype(jnp.int32), axis=1)
    last_local = jnp.clip(group_end - 1 - my_start, 0, shard_rows - 1)
    present = (group_start < my_start + shard_rows) & (group_end > my_start)
    q_piece = lax.all_gather(queries, "seq", axis=0, tiled=True)
    count = q_piece.shape[0]
    q_rows = q_piece.reshape(count * q_piece.shape[1], q_piece.shape[2])
    similar = jnp.einsum("td,rd->tr", q_rows, embedded, preferred_element_type=jnp.float32)
    running = segmented_max(similar, group_id)
    picked = jnp.take(running, last_local, axis=1)
    picked = jnp.where(present[None, :], picked, -jnp.inf)
    part_max = picked.reshape(count, q_piece.shape[1], picked.shape[-1])
    own_count = queries.shape[0]
    token_max = halving_max(part_max, "seq")
    live_mask = (jnp.arange(LQ, dtype=jnp.int32)[None, :] < query_lengths[:, None]).astype(
        jnp.float32
    )
    scores = (
        jnp.sum(token_max * live_mask[:, :, None], axis=1)
        / query_lengths.astype(jnp.float32)[:, None]
    )
    student_scores = scores / SOFTMAX_TEMP
    student_scores = student_scores - jnp.max(student_scores, axis=-1, keepdims=True)
    student_log_prob = student_scores - jnp.log(
        jnp.sum(jnp.exp(student_scores), axis=-1, keepdims=True)
    )
    target_scores = teacher / SOFTMAX_TEMP
    target_scores = target_scores - jnp.max(target_scores, axis=-1, keepdims=True)
    log_t = target_scores - jnp.log(jnp.sum(jnp.exp(target_scores), axis=-1, keepdims=True))
    teacher_prob = jnp.exp(log_t)
    kl_terms = jnp.sum(teacher_prob * (log_t - student_log_prob), axis=-1)
    query_count_all = own_count * seq_count * lax.axis_size("pb")
    loss_sum = butterfly_sum(butterfly_sum(jnp.sum(kl_terms), "seq"), "pb")
    distill_loss = loss_sum / query_count_all
    score_gradient = (jnp.exp(student_log_prob) - teacher_prob) / (SOFTMAX_TEMP * query_count_all)
    return (embedded, scores, score_gradient, distill_loss)


def solution(mesh):
    placed = (
        P("seq", None),
        P(None, "pb"),
        P(None, "pb"),
        P(None, "pb"),
        P("pb", None),
        P(),
        P(),
        P(("seq", "pb"), None, None),
        P(("seq", "pb")),
        P(),
        P(("seq", "pb"), None),
    )

    return jax.shard_map(
        per_device,
        mesh=mesh,
        in_specs=placed,
        out_specs=(P("seq", None), P(("seq", "pb"), None), P(("seq", "pb"), None), P()),
        check_vma=False,
    )
```

```python
import jax
import jax.numpy as jnp
from jax import lax
from jax.sharding import PartitionSpec as P


HD = 128
WIN = 2048
LQ = 32


EPSILON = 1e-06
SOFTMAX_TEMP = 0.1


def sided_fetch(x, axis, distance):
    count = lax.axis_size(axis)
    pairs = []
    for target in range(count):
        source = target - distance if target % 2 == 0 else target + distance
        if 0 <= source < count:
            pairs.append((source, target))
    return lax.ppermute(x, axis, pairs)


def joint_fetch(x, seq_count, pb_count, source_of):
    pairs = []
    for s in range(seq_count):
        for p in range(pb_count):
            from_s, from_p = source_of(s, p)
            pairs.append((from_s * pb_count + from_p, s * pb_count + p))
    return lax.ppermute(x, ("seq", "pb"), pairs)


def xor_swap(x, axis, bit):
    count = lax.axis_size(axis)
    return lax.ppermute(x, axis, [(i, i ^ bit) for i in range(count)])


def ring_shift(x, axis, by):
    count = lax.axis_size(axis)
    return lax.ppermute(x, axis, [(i, (i + by) % count) for i in range(count)])


HALVING_BITS = (1, 2, 16, 4, 32, 8)


def halving_max(values, axis, steps):
    place = lax.axis_index(axis)
    rows = values.shape[0]
    width = rows.bit_length() - 1
    bits = [b for b in HALVING_BITS if b < rows]
    split = values.reshape((2,) * width + values.shape[1:])
    order = [width - 1 - (b.bit_length() - 1) for b in bits]
    split = jnp.transpose(split, order + list(range(width, split.ndim)))
    values = split.reshape((rows,) + values.shape[1:])
    for bit in bits[:steps]:
        half = values.shape[0] // 2
        mine = ((place & bit) != 0).astype(jnp.int32)
        keep = lax.dynamic_slice_in_dim(values, mine * half, half, 0)
        send = lax.dynamic_slice_in_dim(values, (1 - mine) * half, half, 0)
        values = jnp.maximum(keep, xor_swap(send, axis, bit))
    return values


def butterfly_sum(value, axis, bits=None):
    count = lax.axis_size(axis)
    if bits is None:
        bits = [b for b in HALVING_BITS if b < count]
    for bit in bits:
        value = value + xor_swap(value, axis, bit)
    return value


def rms_scale(values, gain):
    mean_sq = jnp.mean(values * values, axis=-1, keepdims=True)
    return values * lax.rsqrt(mean_sq + EPSILON) * gain


def segmented_max(values, group_id):
    span_len = values.shape[-1]
    stride = 1
    while stride < span_len:
        filler = jnp.full(values.shape[:-1] + (stride,), -jnp.inf, values.dtype)
        shifted = jnp.concatenate([filler, values[..., :-stride]], axis=-1)
        prior_id = jnp.concatenate([jnp.full((stride,), -1, jnp.int32), group_id[:-stride]])
        values = jnp.where((prior_id == group_id)[None, :], jnp.maximum(values, shifted), values)
        stride = stride * 2
    return values


def per_device(
    tokens,
    w_query,
    w_key,
    w_value,
    w_out,
    gain_attn,
    gain_embed,
    queries,
    query_lengths,
    group_lengths,
    teacher,
):
    shard_rows = tokens.shape[0]
    seq_count = lax.axis_size("seq")
    seq_place = lax.axis_index("seq")
    head_width = w_query.shape[1]
    heads_here = head_width // HD
    half_win = WIN // 2
    reach_count = half_win // shard_rows
    my_start = seq_place * shard_rows
    total_tokens = shard_rows * seq_count
    residual = tokens.astype(jnp.float32)
    normed = rms_scale(residual, gain_attn).astype(jnp.bfloat16)
    pb_count = lax.axis_size("pb")
    pb_place = lax.axis_index("pb")
    core = seq_place % 2
    block_rows = w_out.shape[0]
    half_rows = block_rows // 2
    w_side = joint_fetch(
        w_out, seq_count, pb_count, lambda s, p: (s, (p + 1 - 2 * (s % 2)) % pb_count)
    )
    w_far = joint_fetch(
        lax.dynamic_slice_in_dim(w_out, core * half_rows, half_rows, 0),
        seq_count,
        pb_count,
        lambda s, p: (s, (p + 2) % pb_count),
    )
    q_local = jnp.dot(normed, w_query, preferred_element_type=jnp.float32).astype(jnp.bfloat16)
    k_local = jnp.dot(normed, w_key, preferred_element_type=jnp.float32).astype(jnp.bfloat16)
    v_local = jnp.dot(normed, w_value, preferred_element_type=jnp.float32).astype(jnp.bfloat16)
    toward = 2 * core - 1
    k_heads_local = k_local.reshape(shard_rows, heads_here, HD).transpose(1, 0, 2)
    v_heads_local = v_local.reshape(shard_rows, heads_here, HD).transpose(1, 0, 2)
    key_value = jnp.stack([k_heads_local, v_heads_local])
    fetched = [sided_fetch(key_value, "seq", d) for d in range(1, reach_count + 1)]
    handed = lax.ppermute(
        jnp.stack([key_value] + fetched[: reach_count - 1]),
        "seq",
        [(i, i ^ 1) for i in range(seq_count)],
    )
    blocks = [key_value] + fetched + [handed[j] for j in range(reach_count)]
    window = jnp.concatenate(blocks, axis=2)
    span_rows = window.shape[2]
    block_shift = jnp.asarray(
        [0] + list(range(1, reach_count + 1)) + [-d for d in range(1, reach_count + 1)], jnp.int32
    )
    block_start = (seq_place + toward * block_shift) * shard_rows
    q_pos = my_start + jnp.arange(shard_rows, dtype=jnp.int32)
    k_pos = (block_start[:, None] + jnp.arange(shard_rows, dtype=jnp.int32)[None, :]).reshape(span_rows)
    in_window = (
        (jnp.abs(q_pos[:, None] - k_pos[None, :]) <= half_win)
        & (k_pos >= 0)[None, :]
        & (k_pos < total_tokens)[None, :]
    )
    q_heads = q_local.reshape(shard_rows, heads_here, HD).transpose(1, 0, 2)
    k_heads = window[0]
    v_heads = window[1]
    logits = jnp.einsum(
        "hqd,hkd->hqk", q_heads, k_heads, preferred_element_type=jnp.float32
    ) * HD ** (-0.5)
    logits = jnp.where(in_window[None], logits, -jnp.inf)
    row_max = jnp.max(logits, axis=-1, keepdims=True)
    exp_terms = jnp.exp(logits - row_max)
    weights = (exp_terms / jnp.sum(exp_terms, axis=-1, keepdims=True)).astype(jnp.bfloat16)
    w_sib = lax.ppermute(
        jnp.concatenate([w_side, w_far], axis=0), "seq", [(i, i ^ 1) for i in range(seq_count)]
    )
    mixed = jnp.einsum("hqk,hkd->qhd", weights, v_heads, preferred_element_type=jnp.float32)
    mixed = mixed.reshape(shard_rows, head_width).astype(jnp.bfloat16)
    mixed_all = jnp.zeros((shard_rows, block_rows * pb_count), mixed.dtype)
    mixed_all = lax.dynamic_update_slice_in_dim(mixed_all, mixed, pb_place * block_rows, 1)
    for k in range(1, pb_count):
        owner = (pb_place - k) % pb_count
        mixed_all = lax.dynamic_update_slice_in_dim(
            mixed_all, ring_shift(mixed, "pb", k), owner * block_rows, 1
        )
    far_owner = (pb_place + 2) % pb_count
    w_all = jnp.zeros((block_rows * pb_count, w_out.shape[1]), w_out.dtype)
    w_all = lax.dynamic_update_slice_in_dim(w_all, w_out, pb_place * block_rows, 0)
    w_all = lax.dynamic_update_slice_in_dim(
        w_all, w_side, ((pb_place + 1 - 2 * core) % pb_count) * block_rows, 0
    )
    w_all = lax.dynamic_update_slice_in_dim(
        w_all, w_sib[:block_rows], ((pb_place - 1 + 2 * core) % pb_count) * block_rows, 0
    )
    w_all = lax.dynamic_update_slice_in_dim(
        w_all, w_far, far_owner * block_rows + core * half_rows, 0
    )
    w_all = lax.dynamic_update_slice_in_dim(
        w_all, w_sib[block_rows:], far_owner * block_rows + (1 - core) * half_rows, 0
    )
    attn_sum = jnp.dot(mixed_all, w_all, preferred_element_type=jnp.float32)
    embedded = rms_scale(residual + attn_sum, gain_embed).astype(jnp.bfloat16)
    group_end = jnp.cumsum(group_lengths)
    group_start = group_end - group_lengths
    group_id = jnp.sum((group_end[None, :] <= q_pos[:, None]).astype(jnp.int32), axis=1)
    last_local = jnp.clip(group_end - 1 - my_start, 0, shard_rows - 1)
    present = (group_start < my_start + shard_rows) & (group_end > my_start)
    q_piece = lax.all_gather(queries, "seq", axis=0, tiled=True)
    count = q_piece.shape[0]
    q_rows = q_piece.reshape(count * q_piece.shape[1], q_piece.shape[2])
    similar = jnp.einsum("td,rd->tr", q_rows, embedded, preferred_element_type=jnp.float32)
    running = segmented_max(similar, group_id)
    picked = jnp.take(running, last_local, axis=1)
    picked = jnp.where(present[None, :], picked, -jnp.inf)
    part_max = picked.reshape(count, q_piece.shape[1], picked.shape[-1])
    own_count = queries.shape[0]
    group_bits = HALVING_BITS[3:]
    token_max = halving_max(part_max, "seq", len(HALVING_BITS) - len(group_bits))
    for bit in group_bits:
        token_max = jnp.maximum(token_max, xor_swap(token_max, "seq", bit))
    side_row = jnp.concatenate([teacher, query_lengths.astype(jnp.float32)[:, None]], axis=1)
    member = 0
    for bit in group_bits:
        member = member * 2 + ((seq_place & bit) != 0).astype(jnp.int32)
    side_parts = [side_row]
    for offset in range(1, 2 ** len(group_bits)):
        mask = 0
        for place, bit in enumerate(group_bits[::-1]):
            if (offset >> place) & 1:
                mask |= bit
        side_parts.append(xor_swap(side_row, "seq", mask))
    side_stack = jnp.concatenate(side_parts, axis=0)
    side_rows = jnp.take(
        side_stack, member ^ jnp.arange(2 ** len(group_bits), dtype=jnp.int32), axis=0
    )
    group_teacher = side_rows[:, :-1]
    group_lengths_f = side_rows[:, -1]
    live_mask = (
        jnp.arange(LQ, dtype=jnp.int32)[None, :] < group_lengths_f.astype(jnp.int32)[:, None]
    ).astype(jnp.float32)
    group_scores = jnp.sum(token_max * live_mask[:, :, None], axis=1) / group_lengths_f[:, None]
    student_scores = group_scores / SOFTMAX_TEMP
    student_scores = student_scores - jnp.max(student_scores, axis=-1, keepdims=True)
    student_log_prob = student_scores - jnp.log(
        jnp.sum(jnp.exp(student_scores), axis=-1, keepdims=True)
    )
    target_scores = group_teacher / SOFTMAX_TEMP
    target_scores = target_scores - jnp.max(target_scores, axis=-1, keepdims=True)
    log_t = target_scores - jnp.log(jnp.sum(jnp.exp(target_scores), axis=-1, keepdims=True))
    teacher_prob = jnp.exp(log_t)
    kl_terms = jnp.sum(teacher_prob * (log_t - student_log_prob), axis=-1)
    query_count_all = own_count * seq_count * lax.axis_size("pb")
    loss_sum = butterfly_sum(butterfly_sum(jnp.sum(kl_terms), "seq", HALVING_BITS[:3]), "pb")
    distill_loss = loss_sum / query_count_all
    gradient_rows = (jnp.exp(student_log_prob) - teacher_prob) / (SOFTMAX_TEMP * query_count_all)
    scores = lax.dynamic_slice_in_dim(group_scores, member, 1, 0)
    score_gradient = lax.dynamic_slice_in_dim(gradient_rows, member, 1, 0)
    return (embedded, scores, score_gradient, distill_loss)


def solution(mesh):
    placed = (
        P("seq", None),
        P(None, "pb"),
        P(None, "pb"),
        P(None, "pb"),
        P("pb", None),
        P(),
        P(),
        P(("seq", "pb"), None, None),
        P(("seq", "pb")),
        P(),
        P(("seq", "pb"), None),
    )

    return jax.shard_map(
        per_device,
        mesh=mesh,
        in_specs=placed,
        out_specs=(P("seq", None), P(("seq", "pb"), None), P(("seq", "pb"), None), P()),
        check_vma=False,
    )
```

```python
import jax
import jax.numpy as jnp
from jax import lax
from jax.sharding import PartitionSpec as P


HD = 128
WIN = 2048
LQ = 32


EPSILON = 1e-06
SOFTMAX_TEMP = 0.1


def sided_fetch(x, axis, distance):
    count = lax.axis_size(axis)
    pairs = []
    for target in range(count):
        source = target - distance if target % 2 == 0 else target + distance
        if 0 <= source < count:
            pairs.append((source, target))
    return lax.ppermute(x, axis, pairs)


def joint_fetch(x, seq_count, pb_count, source_of):
    pairs = []
    for s in range(seq_count):
        for p in range(pb_count):
            from_s, from_p = source_of(s, p)
            pairs.append((from_s * pb_count + from_p, s * pb_count + p))
    return lax.ppermute(x, ("seq", "pb"), pairs)


def xor_swap(x, axis, bit):
    count = lax.axis_size(axis)
    return lax.ppermute(x, axis, [(i, i ^ bit) for i in range(count)])


def ring_shift(x, axis, by):
    count = lax.axis_size(axis)
    return lax.ppermute(x, axis, [(i, (i + by) % count) for i in range(count)])


HALVING_BITS = (1, 2, 16, 4, 32, 8)


def halving_max(values, axis, steps):
    place = lax.axis_index(axis)
    rows = values.shape[0]
    width = rows.bit_length() - 1
    bits = [b for b in HALVING_BITS if b < rows]
    split = values.reshape((2,) * width + values.shape[1:])
    order = [width - 1 - (b.bit_length() - 1) for b in bits]
    split = jnp.transpose(split, order + list(range(width, split.ndim)))
    values = split.reshape((rows,) + values.shape[1:])
    for bit in bits[:steps]:
        half = values.shape[0] // 2
        mine = ((place & bit) != 0).astype(jnp.int32)
        keep = lax.dynamic_slice_in_dim(values, mine * half, half, 0)
        send = lax.dynamic_slice_in_dim(values, (1 - mine) * half, half, 0)
        values = jnp.maximum(keep, xor_swap(send, axis, bit))
    return values


def butterfly_sum(value, axis, bits=None):
    count = lax.axis_size(axis)
    if bits is None:
        bits = [b for b in HALVING_BITS if b < count]
    for bit in bits:
        value = value + xor_swap(value, axis, bit)
    return value


def rms_scale(values, gain):
    mean_sq = jnp.mean(values * values, axis=-1, keepdims=True)
    return values * lax.rsqrt(mean_sq + EPSILON) * gain


def segmented_max(values, group_id):
    span_len = values.shape[-1]
    stride = 1
    while stride < span_len:
        filler = jnp.full(values.shape[:-1] + (stride,), -jnp.inf, values.dtype)
        shifted = jnp.concatenate([filler, values[..., :-stride]], axis=-1)
        prior_id = jnp.concatenate([jnp.full((stride,), -1, jnp.int32), group_id[:-stride]])
        values = jnp.where((prior_id == group_id)[None, :], jnp.maximum(values, shifted), values)
        stride = stride * 2
    return values


def per_device(
    tokens,
    w_query,
    w_key,
    w_value,
    w_out,
    gain_attn,
    gain_embed,
    queries,
    query_lengths,
    group_lengths,
    teacher,
):
    shard_rows = tokens.shape[0]
    seq_count = lax.axis_size("seq")
    seq_place = lax.axis_index("seq")
    head_width = w_query.shape[1]
    heads_here = head_width // HD
    half_win = WIN // 2
    reach_count = half_win // shard_rows
    my_start = seq_place * shard_rows
    total_tokens = shard_rows * seq_count
    residual = tokens.astype(jnp.float32)
    normed = rms_scale(residual, gain_attn).astype(jnp.bfloat16)
    pb_count = lax.axis_size("pb")
    core = seq_place % 2
    half_rows = w_out.shape[0] // 2
    w_side = joint_fetch(
        w_out, seq_count, pb_count, lambda s, p: (s, (p + 1 - 2 * (s % 2)) % pb_count)
    )
    w_far = joint_fetch(
        lax.dynamic_slice_in_dim(w_out, core * half_rows, half_rows, 0),
        seq_count,
        pb_count,
        lambda s, p: (s, (p + 2) % pb_count),
    )
    w_early = jnp.concatenate([w_out, w_side, w_far], axis=0)
    q_local = jnp.dot(normed, w_query, preferred_element_type=jnp.float32).astype(jnp.bfloat16)
    k_local = jnp.dot(normed, w_key, preferred_element_type=jnp.float32).astype(jnp.bfloat16)
    v_local = jnp.dot(normed, w_value, preferred_element_type=jnp.float32).astype(jnp.bfloat16)
    toward = 2 * core - 1
    k_heads_local = k_local.reshape(shard_rows, heads_here, HD).transpose(1, 0, 2)
    v_heads_local = v_local.reshape(shard_rows, heads_here, HD).transpose(1, 0, 2)
    key_value = jnp.stack([k_heads_local, v_heads_local])
    fetched = [sided_fetch(key_value, "seq", d) for d in range(1, reach_count + 1)]
    handed = lax.ppermute(
        jnp.stack([key_value] + fetched[: reach_count - 1]),
        "seq",
        [(i, i ^ 1) for i in range(seq_count)],
    )
    blocks = [key_value] + fetched + [handed[j] for j in range(reach_count)]
    window = jnp.concatenate(blocks, axis=2)
    span_rows = window.shape[2]
    block_shift = jnp.asarray(
        [0] + list(range(1, reach_count + 1)) + [-d for d in range(1, reach_count + 1)], jnp.int32
    )
    block_start = (seq_place + toward * block_shift) * shard_rows
    q_pos = my_start + jnp.arange(shard_rows, dtype=jnp.int32)
    k_pos = (block_start[:, None] + jnp.arange(shard_rows, dtype=jnp.int32)[None, :]).reshape(span_rows)
    in_window = (
        (jnp.abs(q_pos[:, None] - k_pos[None, :]) <= half_win)
        & (k_pos >= 0)[None, :]
        & (k_pos < total_tokens)[None, :]
    )
    q_heads = q_local.reshape(shard_rows, heads_here, HD).transpose(1, 0, 2)
    k_heads = window[0]
    v_heads = window[1]
    logits = jnp.einsum(
        "hqd,hkd->hqk", q_heads, k_heads, preferred_element_type=jnp.float32
    ) * HD ** (-0.5)
    logits = jnp.where(in_window[None], logits, -jnp.inf)
    row_max = jnp.max(logits, axis=-1, keepdims=True)
    exp_terms = jnp.exp(logits - row_max)
    weights = (exp_terms / jnp.sum(exp_terms, axis=-1, keepdims=True)).astype(jnp.bfloat16)
    w_sib = lax.ppermute(
        jnp.concatenate([w_side, w_far], axis=0), "seq", [(i, i ^ 1) for i in range(seq_count)]
    )
    mixed = jnp.einsum("hqk,hkd->qhd", weights, v_heads, preferred_element_type=jnp.float32)
    mixed = mixed.reshape(shard_rows, head_width).astype(jnp.bfloat16)
    from_prev, from_far, from_next = [ring_shift(mixed, "pb", k) for k in range(1, pb_count)]
    first_core = core == 0
    far_lo, far_hi = from_far[:, :half_rows], from_far[:, half_rows:]
    mixed_early = jnp.concatenate(
        [mixed, jnp.where(first_core, from_next, from_prev), jnp.where(first_core, far_lo, far_hi)],
        axis=1,
    )
    mixed_late = jnp.concatenate(
        [jnp.where(first_core, from_prev, from_next), jnp.where(first_core, far_hi, far_lo)], axis=1
    )
    attn_sum = jnp.dot(mixed_early, w_early, preferred_element_type=jnp.float32) + jnp.dot(
        mixed_late, w_sib, preferred_element_type=jnp.float32
    )
    embedded = rms_scale(residual + attn_sum, gain_embed).astype(jnp.bfloat16)
    group_end = jnp.cumsum(group_lengths)
    group_start = group_end - group_lengths
    group_id = jnp.sum((group_end[None, :] <= q_pos[:, None]).astype(jnp.int32), axis=1)
    last_local = jnp.clip(group_end - 1 - my_start, 0, shard_rows - 1)
    present = (group_start < my_start + shard_rows) & (group_end > my_start)
    q_piece = lax.all_gather(queries, "seq", axis=0, tiled=True)
    count = q_piece.shape[0]
    q_rows = q_piece.reshape(count * q_piece.shape[1], q_piece.shape[2])
    similar = jnp.einsum("td,rd->tr", q_rows, embedded, preferred_element_type=jnp.float32)
    running = segmented_max(similar, group_id)
    picked = jnp.take(running, last_local, axis=1)
    picked = jnp.where(present[None, :], picked, -jnp.inf)
    part_max = picked.reshape(count, q_piece.shape[1], picked.shape[-1])
    own_count = queries.shape[0]
    group_bits = HALVING_BITS[3:]
    token_max = halving_max(part_max, "seq", len(HALVING_BITS) - len(group_bits))
    for bit in group_bits:
        token_max = jnp.maximum(token_max, xor_swap(token_max, "seq", bit))
    side_row = jnp.concatenate([teacher, query_lengths.astype(jnp.float32)[:, None]], axis=1)
    member = 0
    for bit in group_bits:
        member = member * 2 + ((seq_place & bit) != 0).astype(jnp.int32)
    side_parts = [side_row]
    for offset in range(1, 2 ** len(group_bits)):
        mask = 0
        for place, bit in enumerate(group_bits[::-1]):
            if (offset >> place) & 1:
                mask |= bit
        side_parts.append(xor_swap(side_row, "seq", mask))
    side_stack = jnp.concatenate(side_parts, axis=0)
    side_rows = jnp.take(
        side_stack, member ^ jnp.arange(2 ** len(group_bits), dtype=jnp.int32), axis=0
    )
    group_teacher = side_rows[:, :-1]
    group_lengths_f = side_rows[:, -1]
    live_mask = (
        jnp.arange(LQ, dtype=jnp.int32)[None, :] < group_lengths_f.astype(jnp.int32)[:, None]
    ).astype(jnp.float32)
    group_scores = jnp.sum(token_max * live_mask[:, :, None], axis=1) / group_lengths_f[:, None]
    student_scores = group_scores / SOFTMAX_TEMP
    student_scores = student_scores - jnp.max(student_scores, axis=-1, keepdims=True)
    student_log_prob = student_scores - jnp.log(
        jnp.sum(jnp.exp(student_scores), axis=-1, keepdims=True)
    )
    target_scores = group_teacher / SOFTMAX_TEMP
    target_scores = target_scores - jnp.max(target_scores, axis=-1, keepdims=True)
    log_t = target_scores - jnp.log(jnp.sum(jnp.exp(target_scores), axis=-1, keepdims=True))
    teacher_prob = jnp.exp(log_t)
    kl_terms = jnp.sum(teacher_prob * (log_t - student_log_prob), axis=-1)
    query_count_all = own_count * seq_count * lax.axis_size("pb")
    loss_sum = butterfly_sum(butterfly_sum(jnp.sum(kl_terms), "seq", HALVING_BITS[:3]), "pb")
    distill_loss = loss_sum / query_count_all
    gradient_rows = (jnp.exp(student_log_prob) - teacher_prob) / (SOFTMAX_TEMP * query_count_all)
    scores = lax.dynamic_slice_in_dim(group_scores, member, 1, 0)
    score_gradient = lax.dynamic_slice_in_dim(gradient_rows, member, 1, 0)
    return (embedded, scores, score_gradient, distill_loss)


def solution(mesh):
    placed = (
        P("seq", None),
        P(None, "pb"),
        P(None, "pb"),
        P(None, "pb"),
        P("pb", None),
        P(),
        P(),
        P(("seq", "pb"), None, None),
        P(("seq", "pb")),
        P(),
        P(("seq", "pb"), None),
    )

    return jax.shard_map(
        per_device,
        mesh=mesh,
        in_specs=placed,
        out_specs=(P("seq", None), P(("seq", "pb"), None), P(("seq", "pb"), None), P()),
        check_vma=False,
    )
```

```python
import jax
import jax.numpy as jnp
from jax import lax
from jax.sharding import PartitionSpec as P


HD = 128
WIN = 2048
LQ = 32


EPSILON = 1e-06
SOFTMAX_TEMP = 0.1


def sided_fetch(x, axis, distance):
    count = lax.axis_size(axis)
    pairs = []
    for target in range(count):
        source = target - distance if target % 2 == 0 else target + distance
        if 0 <= source < count:
            pairs.append((source, target))
    return lax.ppermute(x, axis, pairs)


def joint_fetch(x, seq_count, pb_count, source_of):
    pairs = []
    for s in range(seq_count):
        for p in range(pb_count):
            from_s, from_p = source_of(s, p)
            pairs.append((from_s * pb_count + from_p, s * pb_count + p))
    return lax.ppermute(x, ("seq", "pb"), pairs)


def xor_swap(x, axis, bit):
    count = lax.axis_size(axis)
    return lax.ppermute(x, axis, [(i, i ^ bit) for i in range(count)])


def ring_shift(x, axis, by):
    count = lax.axis_size(axis)
    return lax.ppermute(x, axis, [(i, (i + by) % count) for i in range(count)])


HALVING_BITS = (1, 2, 16, 4, 32, 8)


def halving_max(values, axis, steps):
    place = lax.axis_index(axis)
    rows = values.shape[0]
    width = rows.bit_length() - 1
    bits = [b for b in HALVING_BITS if b < rows]
    split = values.reshape((2,) * width + values.shape[1:])
    order = [width - 1 - (b.bit_length() - 1) for b in bits]
    split = jnp.transpose(split, order + list(range(width, split.ndim)))
    values = split.reshape((rows,) + values.shape[1:])
    for bit in bits[:steps]:
        half = values.shape[0] // 2
        mine = ((place & bit) != 0).astype(jnp.int32)
        keep = lax.dynamic_slice_in_dim(values, mine * half, half, 0)
        send = lax.dynamic_slice_in_dim(values, (1 - mine) * half, half, 0)
        values = jnp.maximum(keep, xor_swap(send, axis, bit))
    return values


def butterfly_sum(value, axis, bits=None):
    count = lax.axis_size(axis)
    if bits is None:
        bits = [b for b in HALVING_BITS if b < count]
    for bit in bits:
        value = value + xor_swap(value, axis, bit)
    return value


def rms_scale(values, gain):
    mean_sq = jnp.mean(values * values, axis=-1, keepdims=True)
    return values * lax.rsqrt(mean_sq + EPSILON) * gain


def segmented_max(values, group_id):
    span_len = values.shape[-1]
    stride = 1
    while stride < span_len:
        filler = jnp.full(values.shape[:-1] + (stride,), -jnp.inf, values.dtype)
        shifted = jnp.concatenate([filler, values[..., :-stride]], axis=-1)
        prior_id = jnp.concatenate([jnp.full((stride,), -1, jnp.int32), group_id[:-stride]])
        values = jnp.where((prior_id == group_id)[None, :], jnp.maximum(values, shifted), values)
        stride = stride * 2
    return values


def per_device(
    tokens,
    w_query,
    w_key,
    w_value,
    w_out,
    gain_attn,
    gain_embed,
    queries,
    query_lengths,
    group_lengths,
    teacher,
):
    shard_rows = tokens.shape[0]
    seq_count = lax.axis_size("seq")
    seq_place = lax.axis_index("seq")
    head_width = w_query.shape[1]
    heads_here = head_width // HD
    half_win = WIN // 2
    reach_count = half_win // shard_rows
    my_start = seq_place * shard_rows
    total_tokens = shard_rows * seq_count
    residual = tokens.astype(jnp.float32)
    normed = rms_scale(residual, gain_attn).astype(jnp.bfloat16)
    pb_count = lax.axis_size("pb")
    core = seq_place % 2
    half_rows = w_out.shape[0] // 2
    w_side = joint_fetch(
        w_out, seq_count, pb_count, lambda s, p: (s, (p + 1 - 2 * (s % 2)) % pb_count)
    )
    w_far = joint_fetch(
        lax.dynamic_slice_in_dim(w_out, core * half_rows, half_rows, 0),
        seq_count,
        pb_count,
        lambda s, p: (s, (p + 2) % pb_count),
    )
    w_early = jnp.concatenate([w_out, w_side, w_far], axis=0)
    q_local = jnp.dot(normed, w_query, preferred_element_type=jnp.float32).astype(jnp.bfloat16)
    k_local = jnp.dot(normed, w_key, preferred_element_type=jnp.float32).astype(jnp.bfloat16)
    v_local = jnp.dot(normed, w_value, preferred_element_type=jnp.float32).astype(jnp.bfloat16)
    toward = 2 * core - 1
    k_heads_local = k_local.reshape(shard_rows, heads_here, HD).transpose(1, 0, 2)
    v_heads_local = v_local.reshape(shard_rows, heads_here, HD).transpose(1, 0, 2)
    key_value = jnp.stack([k_heads_local, v_heads_local])
    fetched = [sided_fetch(key_value, "seq", d) for d in range(1, reach_count + 1)]
    handed = lax.ppermute(
        jnp.stack([key_value] + fetched[: reach_count - 1]),
        "seq",
        [(i, i ^ 1) for i in range(seq_count)],
    )
    blocks = [key_value] + fetched + [handed[j] for j in range(reach_count)]
    window = jnp.concatenate(blocks, axis=2)
    span_rows = window.shape[2]
    block_shift = jnp.asarray(
        [0] + list(range(1, reach_count + 1)) + [-d for d in range(1, reach_count + 1)], jnp.int32
    )
    block_start = (seq_place + toward * block_shift) * shard_rows
    q_pos = my_start + jnp.arange(shard_rows, dtype=jnp.int32)
    k_pos = (block_start[:, None] + jnp.arange(shard_rows, dtype=jnp.int32)[None, :]).reshape(span_rows)
    in_window = (
        (jnp.abs(q_pos[:, None] - k_pos[None, :]) <= half_win)
        & (k_pos >= 0)[None, :]
        & (k_pos < total_tokens)[None, :]
    )
    q_heads = q_local.reshape(shard_rows, heads_here, HD).transpose(1, 0, 2)
    k_heads = window[0]
    v_heads = window[1]
    logits = jnp.einsum(
        "hqd,hkd->hqk", q_heads, k_heads, preferred_element_type=jnp.float32
    ) * HD ** (-0.5)
    logits = jnp.where(in_window[None], logits, -jnp.inf)
    row_max = jnp.max(logits, axis=-1, keepdims=True)
    exp_terms = jnp.exp(logits - row_max)
    weights = (exp_terms / jnp.sum(exp_terms, axis=-1, keepdims=True)).astype(jnp.bfloat16)
    w_sib = lax.ppermute(
        jnp.concatenate([w_side, w_far], axis=0), "seq", [(i, i ^ 1) for i in range(seq_count)]
    )
    mixed = jnp.einsum("hqk,hkd->qhd", weights, v_heads, preferred_element_type=jnp.float32)
    mixed = mixed.reshape(shard_rows, head_width).astype(jnp.bfloat16)
    from_prev, from_far, from_next = [ring_shift(mixed, "pb", k) for k in range(1, pb_count)]
    first_core = core == 0
    far_lo, far_hi = from_far[:, :half_rows], from_far[:, half_rows:]
    mixed_early = jnp.concatenate(
        [mixed, jnp.where(first_core, from_next, from_prev), jnp.where(first_core, far_lo, far_hi)],
        axis=1,
    )
    mixed_late = jnp.concatenate(
        [jnp.where(first_core, from_prev, from_next), jnp.where(first_core, far_hi, far_lo)], axis=1
    )
    attn_sum = jnp.dot(mixed_early, w_early, preferred_element_type=jnp.float32) + jnp.dot(
        mixed_late, w_sib, preferred_element_type=jnp.float32
    )
    embedded = rms_scale(residual + attn_sum, gain_embed).astype(jnp.bfloat16)
    group_end = jnp.cumsum(group_lengths)
    group_start = group_end - group_lengths
    group_id = jnp.sum((group_end[None, :] <= q_pos[:, None]).astype(jnp.int32), axis=1)
    last_local = jnp.clip(group_end - 1 - my_start, 0, shard_rows - 1)
    present = (group_start < my_start + shard_rows) & (group_end > my_start)
    q_piece = lax.all_gather(queries, "seq", axis=0, tiled=True)
    count = q_piece.shape[0]
    q_rows = q_piece.reshape(count * q_piece.shape[1], q_piece.shape[2])
    similar = jnp.einsum("td,rd->tr", q_rows, embedded, preferred_element_type=jnp.float32)
    running = segmented_max(similar, group_id)
    picked = jnp.take(running, last_local, axis=1)
    picked = jnp.where(present[None, :], picked, -jnp.inf)
    part_max = picked.reshape(count, q_piece.shape[1], picked.shape[-1])
    own_count = queries.shape[0]
    group_bits = HALVING_BITS[3:]
    token_max = halving_max(part_max, "seq", len(HALVING_BITS) - len(group_bits))
    member = 0
    for bit in group_bits:
        member = member * 2 + ((seq_place & bit) != 0).astype(jnp.int32)
    group_size = 2 ** len(group_bits)
    side_row = jnp.concatenate([teacher, query_lengths.astype(jnp.float32)[:, None]], axis=1)
    side_rows = jnp.where(
        (jnp.arange(group_size, dtype=jnp.int32) == member)[:, None],
        jnp.broadcast_to(side_row, (group_size, side_row.shape[1])),
        -jnp.inf,
    )
    slot_width = token_max.shape[1] * token_max.shape[2]
    packed = jnp.concatenate([token_max.reshape(group_size, slot_width), side_rows], axis=1)
    for bit in group_bits:
        packed = jnp.maximum(packed, xor_swap(packed, "seq", bit))
    token_max = packed[:, :slot_width].reshape(group_size, *part_max.shape[1:])
    side_rows = packed[:, slot_width:]
    group_teacher = side_rows[:, :-1]
    group_lengths_f = side_rows[:, -1]
    live_mask = (
        jnp.arange(LQ, dtype=jnp.int32)[None, :] < group_lengths_f.astype(jnp.int32)[:, None]
    ).astype(jnp.float32)
    group_scores = jnp.sum(token_max * live_mask[:, :, None], axis=1) / group_lengths_f[:, None]
    student_scores = group_scores / SOFTMAX_TEMP
    student_scores = student_scores - jnp.max(student_scores, axis=-1, keepdims=True)
    student_log_prob = student_scores - jnp.log(
        jnp.sum(jnp.exp(student_scores), axis=-1, keepdims=True)
    )
    target_scores = group_teacher / SOFTMAX_TEMP
    target_scores = target_scores - jnp.max(target_scores, axis=-1, keepdims=True)
    log_t = target_scores - jnp.log(jnp.sum(jnp.exp(target_scores), axis=-1, keepdims=True))
    teacher_prob = jnp.exp(log_t)
    kl_terms = jnp.sum(teacher_prob * (log_t - student_log_prob), axis=-1)
    query_count_all = own_count * seq_count * lax.axis_size("pb")
    loss_sum = butterfly_sum(butterfly_sum(jnp.sum(kl_terms), "seq", HALVING_BITS[:3]), "pb")
    distill_loss = loss_sum / query_count_all
    gradient_rows = (jnp.exp(student_log_prob) - teacher_prob) / (SOFTMAX_TEMP * query_count_all)
    scores = lax.dynamic_slice_in_dim(group_scores, member, 1, 0)
    score_gradient = lax.dynamic_slice_in_dim(gradient_rows, member, 1, 0)
    return (embedded, scores, score_gradient, distill_loss)


def solution(mesh):
    placed = (
        P("seq", None),
        P(None, "pb"),
        P(None, "pb"),
        P(None, "pb"),
        P("pb", None),
        P(),
        P(),
        P(("seq", "pb"), None, None),
        P(("seq", "pb")),
        P(),
        P(("seq", "pb"), None),
    )

    return jax.shard_map(
        per_device,
        mesh=mesh,
        in_specs=placed,
        out_specs=(P("seq", None), P(("seq", "pb"), None), P(("seq", "pb"), None), P()),
        check_vma=False,
    )
```

```python
import jax
import jax.numpy as jnp
from jax import lax
from jax.sharding import PartitionSpec as P


HD = 128
WIN = 2048
LQ = 32


EPSILON = 1e-06
SOFTMAX_TEMP = 0.1


def sided_fetch(x, axis, distance):
    count = lax.axis_size(axis)
    pairs = []
    for target in range(count):
        source = target - distance if target % 2 == 0 else target + distance
        if 0 <= source < count:
            pairs.append((source, target))
    return lax.ppermute(x, axis, pairs)


def xor_swap(x, axis, bit):
    count = lax.axis_size(axis)
    return lax.ppermute(x, axis, [(i, i ^ bit) for i in range(count)])


def ring_shift(x, axis, by):
    count = lax.axis_size(axis)
    return lax.ppermute(x, axis, [(i, (i + by) % count) for i in range(count)])


HALVING_BITS = (1, 2, 16, 4, 32, 8)


def halving_max(values, axis, steps):
    place = lax.axis_index(axis)
    rows = values.shape[0]
    width = rows.bit_length() - 1
    bits = [b for b in HALVING_BITS if b < rows]
    split = values.reshape((2,) * width + values.shape[1:])
    order = [width - 1 - (b.bit_length() - 1) for b in bits]
    split = jnp.transpose(split, order + list(range(width, split.ndim)))
    values = split.reshape((rows,) + values.shape[1:])
    for bit in bits[:steps]:
        half = values.shape[0] // 2
        mine = ((place & bit) != 0).astype(jnp.int32)
        keep = lax.dynamic_slice_in_dim(values, mine * half, half, 0)
        send = lax.dynamic_slice_in_dim(values, (1 - mine) * half, half, 0)
        values = jnp.maximum(keep, xor_swap(send, axis, bit))
    return values


def butterfly_sum(value, axis, bits=None):
    count = lax.axis_size(axis)
    if bits is None:
        bits = [b for b in HALVING_BITS if b < count]
    for bit in bits:
        value = value + xor_swap(value, axis, bit)
    return value


def rms_scale(values, gain):
    mean_sq = jnp.mean(values * values, axis=-1, keepdims=True)
    return values * lax.rsqrt(mean_sq + EPSILON) * gain


def segmented_max(values, group_id):
    span_len = values.shape[-1]
    stride = 1
    while stride < span_len:
        filler = jnp.full(values.shape[:-1] + (stride,), -jnp.inf, values.dtype)
        shifted = jnp.concatenate([filler, values[..., :-stride]], axis=-1)
        prior_id = jnp.concatenate([jnp.full((stride,), -1, jnp.int32), group_id[:-stride]])
        values = jnp.where((prior_id == group_id)[None, :], jnp.maximum(values, shifted), values)
        stride = stride * 2
    return values


def per_device(
    tokens,
    w_query,
    w_key,
    w_value,
    w_out,
    gain_attn,
    gain_embed,
    queries,
    query_lengths,
    group_lengths,
    teacher,
):
    shard_rows = tokens.shape[0]
    seq_count = lax.axis_size("seq")
    seq_place = lax.axis_index("seq")
    head_width = w_query.shape[1]
    heads_here = head_width // HD
    half_win = WIN // 2
    reach_count = half_win // shard_rows
    my_start = seq_place * shard_rows
    total_tokens = shard_rows * seq_count
    residual = tokens.astype(jnp.float32)
    normed = rms_scale(residual, gain_attn).astype(jnp.bfloat16)
    pb_count = lax.axis_size("pb")
    w_out_parts = [w_out] + [ring_shift(w_out, "pb", k) for k in range(1, pb_count)]
    q_local = jnp.dot(normed, w_query, preferred_element_type=jnp.float32).astype(jnp.bfloat16)
    k_local = jnp.dot(normed, w_key, preferred_element_type=jnp.float32).astype(jnp.bfloat16)
    v_local = jnp.dot(normed, w_value, preferred_element_type=jnp.float32).astype(jnp.bfloat16)
    core = seq_place % 2
    toward = 2 * core - 1
    k_heads_local = k_local.reshape(shard_rows, heads_here, HD).transpose(1, 0, 2)
    v_heads_local = v_local.reshape(shard_rows, heads_here, HD).transpose(1, 0, 2)
    key_value = jnp.stack([k_heads_local, v_heads_local])
    fetched = [sided_fetch(key_value, "seq", d) for d in range(1, reach_count + 1)]
    handed = lax.ppermute(
        jnp.stack([key_value] + fetched[: reach_count - 1]),
        "seq",
        [(i, i ^ 1) for i in range(seq_count)],
    )
    blocks = [key_value] + fetched + [handed[j] for j in range(reach_count)]
    window = jnp.concatenate(blocks, axis=2)
    span_rows = window.shape[2]
    block_shift = jnp.asarray(
        [0] + list(range(1, reach_count + 1)) + [-d for d in range(1, reach_count + 1)], jnp.int32
    )
    block_start = (seq_place + toward * block_shift) * shard_rows
    q_pos = my_start + jnp.arange(shard_rows, dtype=jnp.int32)
    k_pos = (block_start[:, None] + jnp.arange(shard_rows, dtype=jnp.int32)[None, :]).reshape(span_rows)
    in_window = (
        (jnp.abs(q_pos[:, None] - k_pos[None, :]) <= half_win)
        & (k_pos >= 0)[None, :]
        & (k_pos < total_tokens)[None, :]
    )
    q_heads = q_local.reshape(shard_rows, heads_here, HD).transpose(1, 0, 2)
    k_heads = window[0]
    v_heads = window[1]
    logits = jnp.einsum(
        "hqd,hkd->hqk", q_heads, k_heads, preferred_element_type=jnp.float32
    ) * HD ** (-0.5)
    logits = jnp.where(in_window[None], logits, -jnp.inf)
    row_max = jnp.max(logits, axis=-1, keepdims=True)
    exp_terms = jnp.exp(logits - row_max)
    weights = (exp_terms / jnp.sum(exp_terms, axis=-1, keepdims=True)).astype(jnp.bfloat16)
    mixed = jnp.einsum("hqk,hkd->qhd", weights, v_heads, preferred_element_type=jnp.float32)
    mixed = mixed.reshape(shard_rows, head_width).astype(jnp.bfloat16)
    mixed_parts = [mixed] + [ring_shift(mixed, "pb", k) for k in range(1, pb_count)]
    attn_sum = jnp.dot(
        jnp.concatenate(mixed_parts, axis=1),
        jnp.concatenate(w_out_parts, axis=0),
        preferred_element_type=jnp.float32,
    )
    embedded = rms_scale(residual + attn_sum, gain_embed).astype(jnp.bfloat16)
    group_end = jnp.cumsum(group_lengths)
    group_start = group_end - group_lengths
    group_id = jnp.sum((group_end[None, :] <= q_pos[:, None]).astype(jnp.int32), axis=1)
    last_local = jnp.clip(group_end - 1 - my_start, 0, shard_rows - 1)
    present = (group_start < my_start + shard_rows) & (group_end > my_start)
    q_piece = lax.all_gather(queries, "seq", axis=0, tiled=True)
    count = q_piece.shape[0]
    q_rows = q_piece.reshape(count * q_piece.shape[1], q_piece.shape[2])
    similar = jnp.einsum("td,rd->tr", q_rows, embedded, preferred_element_type=jnp.float32)
    running = segmented_max(similar, group_id)
    picked = jnp.take(running, last_local, axis=1)
    picked = jnp.where(present[None, :], picked, -jnp.inf)
    part_max = picked.reshape(count, q_piece.shape[1], picked.shape[-1])
    own_count = queries.shape[0]
    group_bits = HALVING_BITS[3:]
    token_max = halving_max(part_max, "seq", len(HALVING_BITS) - len(group_bits))
    member = 0
    for bit in group_bits:
        member = member * 2 + ((seq_place & bit) != 0).astype(jnp.int32)
    group_size = 2 ** len(group_bits)
    side_row = jnp.concatenate([teacher, query_lengths.astype(jnp.float32)[:, None]], axis=1)
    side_rows = jnp.where(
        (jnp.arange(group_size, dtype=jnp.int32) == member)[:, None],
        jnp.broadcast_to(side_row, (group_size, side_row.shape[1])),
        -jnp.inf,
    )
    slot_width = token_max.shape[1] * token_max.shape[2]
    packed = jnp.concatenate([token_max.reshape(group_size, slot_width), side_rows], axis=1)
    for bit in group_bits:
        packed = jnp.maximum(packed, xor_swap(packed, "seq", bit))
    token_max = packed[:, :slot_width].reshape(group_size, *part_max.shape[1:])
    side_rows = packed[:, slot_width:]
    group_teacher = side_rows[:, :-1]
    group_lengths_f = side_rows[:, -1]
    live_mask = (
        jnp.arange(LQ, dtype=jnp.int32)[None, :] < group_lengths_f.astype(jnp.int32)[:, None]
    ).astype(jnp.float32)
    group_scores = jnp.sum(token_max * live_mask[:, :, None], axis=1) / group_lengths_f[:, None]
    student_scores = group_scores / SOFTMAX_TEMP
    student_scores = student_scores - jnp.max(student_scores, axis=-1, keepdims=True)
    student_log_prob = student_scores - jnp.log(
        jnp.sum(jnp.exp(student_scores), axis=-1, keepdims=True)
    )
    target_scores = group_teacher / SOFTMAX_TEMP
    target_scores = target_scores - jnp.max(target_scores, axis=-1, keepdims=True)
    log_t = target_scores - jnp.log(jnp.sum(jnp.exp(target_scores), axis=-1, keepdims=True))
    teacher_prob = jnp.exp(log_t)
    kl_terms = jnp.sum(teacher_prob * (log_t - student_log_prob), axis=-1)
    query_count_all = own_count * seq_count * lax.axis_size("pb")
    loss_sum = butterfly_sum(butterfly_sum(jnp.sum(kl_terms), "seq", HALVING_BITS[:3]), "pb")
    distill_loss = loss_sum / query_count_all
    gradient_rows = (jnp.exp(student_log_prob) - teacher_prob) / (SOFTMAX_TEMP * query_count_all)
    scores = lax.dynamic_slice_in_dim(group_scores, member, 1, 0)
    score_gradient = lax.dynamic_slice_in_dim(gradient_rows, member, 1, 0)
    return (embedded, scores, score_gradient, distill_loss)


def solution(mesh):
    placed = (
        P("seq", None),
        P(None, "pb"),
        P(None, "pb"),
        P(None, "pb"),
        P("pb", None),
        P(),
        P(),
        P(("seq", "pb"), None, None),
        P(("seq", "pb")),
        P(),
        P(("seq", "pb"), None),
    )

    return jax.shard_map(
        per_device,
        mesh=mesh,
        in_specs=placed,
        out_specs=(P("seq", None), P(("seq", "pb"), None), P(("seq", "pb"), None), P()),
        check_vma=False,
    )
```

```python
import jax
import jax.numpy as jnp
from jax import lax
from jax.sharding import PartitionSpec as P


HD = 128
WIN = 2048
LQ = 32


EPSILON = 1e-06
SOFTMAX_TEMP = 0.1


def sided_fetch(x, axis, distance):
    count = lax.axis_size(axis)
    pairs = []
    for target in range(count):
        source = target - distance if target % 2 == 0 else target + distance
        if 0 <= source < count:
            pairs.append((source, target))
    return lax.ppermute(x, axis, pairs)


def xor_swap(x, axis, bit):
    count = lax.axis_size(axis)
    return lax.ppermute(x, axis, [(i, i ^ bit) for i in range(count)])


def ring_shift(x, axis, by):
    count = lax.axis_size(axis)
    return lax.ppermute(x, axis, [(i, (i + by) % count) for i in range(count)])


HALVING_BITS = (1, 2, 16, 4, 32, 8)


def halving_max(values, axis, steps):
    place = lax.axis_index(axis)
    rows = values.shape[0]
    width = rows.bit_length() - 1
    bits = [b for b in HALVING_BITS if b < rows]
    split = values.reshape((2,) * width + values.shape[1:])
    order = [width - 1 - (b.bit_length() - 1) for b in bits]
    split = jnp.transpose(split, order + list(range(width, split.ndim)))
    values = split.reshape((rows,) + values.shape[1:])
    for bit in bits[:steps]:
        half = values.shape[0] // 2
        mine = ((place & bit) != 0).astype(jnp.int32)
        keep = lax.dynamic_slice_in_dim(values, mine * half, half, 0)
        send = lax.dynamic_slice_in_dim(values, (1 - mine) * half, half, 0)
        values = jnp.maximum(keep, xor_swap(send, axis, bit))
    return values


def butterfly_sum(value, axis, bits=None):
    count = lax.axis_size(axis)
    if bits is None:
        bits = [b for b in HALVING_BITS if b < count]
    for bit in bits:
        value = value + xor_swap(value, axis, bit)
    return value


def rms_scale(values, gain):
    mean_sq = jnp.mean(values * values, axis=-1, keepdims=True)
    return values * lax.rsqrt(mean_sq + EPSILON) * gain


def segmented_max(values, group_id):
    span_len = values.shape[-1]
    stride = 1
    while stride < span_len:
        filler = jnp.full(values.shape[:-1] + (stride,), -jnp.inf, values.dtype)
        shifted = jnp.concatenate([filler, values[..., :-stride]], axis=-1)
        prior_id = jnp.concatenate([jnp.full((stride,), -1, jnp.int32), group_id[:-stride]])
        values = jnp.where((prior_id == group_id)[None, :], jnp.maximum(values, shifted), values)
        stride = stride * 2
    return values


def per_device(
    tokens,
    w_query,
    w_key,
    w_value,
    w_out,
    gain_attn,
    gain_embed,
    queries,
    query_lengths,
    group_lengths,
    teacher,
):
    shard_rows = tokens.shape[0]
    seq_count = lax.axis_size("seq")
    seq_place = lax.axis_index("seq")
    head_width = w_query.shape[1]
    heads_here = head_width // HD
    half_win = WIN // 2
    reach_count = half_win // shard_rows
    my_start = seq_place * shard_rows
    total_tokens = shard_rows * seq_count
    residual = tokens.astype(jnp.float32)
    normed = rms_scale(residual, gain_attn).astype(jnp.bfloat16)
    pb_count = lax.axis_size("pb")
    w_out_parts = [w_out] + [ring_shift(w_out, "pb", k) for k in range(1, pb_count)]
    q_local = jnp.dot(normed, w_query, preferred_element_type=jnp.float32).astype(jnp.bfloat16)
    k_local = jnp.dot(normed, w_key, preferred_element_type=jnp.float32).astype(jnp.bfloat16)
    v_local = jnp.dot(normed, w_value, preferred_element_type=jnp.float32).astype(jnp.bfloat16)
    core = seq_place % 2
    toward = 2 * core - 1
    k_heads_local = k_local.reshape(shard_rows, heads_here, HD).transpose(1, 0, 2)
    v_heads_local = v_local.reshape(shard_rows, heads_here, HD).transpose(1, 0, 2)
    key_value = jnp.stack([k_heads_local, v_heads_local])
    fetched = [sided_fetch(key_value, "seq", d) for d in range(1, reach_count + 1)]
    handed = lax.ppermute(
        jnp.stack([key_value] + fetched[: reach_count - 1]),
        "seq",
        [(i, i ^ 1) for i in range(seq_count)],
    )
    blocks = [key_value] + fetched + [handed[j] for j in range(reach_count)]
    window = jnp.concatenate(blocks, axis=2)
    span_rows = window.shape[2]
    block_shift = jnp.asarray(
        [0] + list(range(1, reach_count + 1)) + [-d for d in range(1, reach_count + 1)], jnp.int32
    )
    block_start = (seq_place + toward * block_shift) * shard_rows
    q_pos = my_start + jnp.arange(shard_rows, dtype=jnp.int32)
    k_pos = (block_start[:, None] + jnp.arange(shard_rows, dtype=jnp.int32)[None, :]).reshape(span_rows)
    in_window = (
        (jnp.abs(q_pos[:, None] - k_pos[None, :]) <= half_win)
        & (k_pos >= 0)[None, :]
        & (k_pos < total_tokens)[None, :]
    )
    q_heads = q_local.reshape(shard_rows, heads_here, HD).transpose(1, 0, 2)
    k_heads = window[0]
    v_heads = window[1]
    logits = jnp.einsum(
        "hqd,hkd->hqk", q_heads, k_heads, preferred_element_type=jnp.float32
    ) * HD ** (-0.5)
    logits = jnp.where(in_window[None], logits, -jnp.inf)
    row_max = jnp.max(logits, axis=-1, keepdims=True)
    exp_terms = jnp.exp(logits - row_max)
    weights = (exp_terms / jnp.sum(exp_terms, axis=-1, keepdims=True)).astype(jnp.bfloat16)
    mixed = jnp.einsum("hqk,hkd->qhd", weights, v_heads, preferred_element_type=jnp.float32)
    mixed = mixed.reshape(shard_rows, head_width).astype(jnp.bfloat16)
    mixed_parts = [mixed] + [ring_shift(mixed, "pb", k) for k in range(1, pb_count)]
    attn_sum = jnp.dot(
        jnp.concatenate(mixed_parts, axis=1),
        jnp.concatenate(w_out_parts, axis=0),
        preferred_element_type=jnp.float32,
    )
    embedded = rms_scale(residual + attn_sum, gain_embed).astype(jnp.bfloat16)
    group_end = jnp.cumsum(group_lengths)
    group_start = group_end - group_lengths
    group_id = jnp.sum((group_end[None, :] <= q_pos[:, None]).astype(jnp.int32), axis=1)
    last_local = jnp.clip(group_end - 1 - my_start, 0, shard_rows - 1)
    present = (group_start < my_start + shard_rows) & (group_end > my_start)
    q_piece = lax.all_gather(queries, "seq", axis=0, tiled=True)
    count = q_piece.shape[0]
    q_rows = q_piece.reshape(count * q_piece.shape[1], q_piece.shape[2])
    similar = jnp.einsum("td,rd->tr", q_rows, embedded, preferred_element_type=jnp.float32)
    running = segmented_max(similar, group_id)
    picked = jnp.take(running, last_local, axis=1)
    picked = jnp.where(present[None, :], picked, -jnp.inf)
    part_max = picked.reshape(count, q_piece.shape[1], picked.shape[-1])
    own_count = queries.shape[0]
    group_bits = HALVING_BITS[3:]
    token_max = halving_max(part_max, "seq", len(HALVING_BITS) - len(group_bits))
    for bit in group_bits:
        token_max = jnp.maximum(token_max, xor_swap(token_max, "seq", bit))
    side_row = jnp.concatenate([teacher, query_lengths.astype(jnp.float32)[:, None]], axis=1)
    member = 0
    for bit in group_bits:
        member = member * 2 + ((seq_place & bit) != 0).astype(jnp.int32)
    side_parts = [side_row]
    for offset in range(1, 2 ** len(group_bits)):
        mask = 0
        for place, bit in enumerate(group_bits[::-1]):
            if (offset >> place) & 1:
                mask |= bit
        side_parts.append(xor_swap(side_row, "seq", mask))
    side_stack = jnp.concatenate(side_parts, axis=0)
    side_rows = jnp.take(
        side_stack, member ^ jnp.arange(2 ** len(group_bits), dtype=jnp.int32), axis=0
    )
    group_teacher = side_rows[:, :-1]
    group_lengths_f = side_rows[:, -1]
    live_mask = (
        jnp.arange(LQ, dtype=jnp.int32)[None, :] < group_lengths_f.astype(jnp.int32)[:, None]
    ).astype(jnp.float32)
    group_scores = jnp.sum(token_max * live_mask[:, :, None], axis=1) / group_lengths_f[:, None]
    student_scores = group_scores / SOFTMAX_TEMP
    student_scores = student_scores - jnp.max(student_scores, axis=-1, keepdims=True)
    student_log_prob = student_scores - jnp.log(
        jnp.sum(jnp.exp(student_scores), axis=-1, keepdims=True)
    )
    target_scores = group_teacher / SOFTMAX_TEMP
    target_scores = target_scores - jnp.max(target_scores, axis=-1, keepdims=True)
    log_t = target_scores - jnp.log(jnp.sum(jnp.exp(target_scores), axis=-1, keepdims=True))
    teacher_prob = jnp.exp(log_t)
    kl_terms = jnp.sum(teacher_prob * (log_t - student_log_prob), axis=-1)
    query_count_all = own_count * seq_count * lax.axis_size("pb")
    loss_sum = lax.psum(butterfly_sum(jnp.sum(kl_terms), "seq", HALVING_BITS[:3]), "pb")
    distill_loss = loss_sum / query_count_all
    gradient_rows = (jnp.exp(student_log_prob) - teacher_prob) / (SOFTMAX_TEMP * query_count_all)
    scores = lax.dynamic_slice_in_dim(group_scores, member, 1, 0)
    score_gradient = lax.dynamic_slice_in_dim(gradient_rows, member, 1, 0)
    return (embedded, scores, score_gradient, distill_loss)


def solution(mesh):
    placed = (
        P("seq", None),
        P(None, "pb"),
        P(None, "pb"),
        P(None, "pb"),
        P("pb", None),
        P(),
        P(),
        P(("seq", "pb"), None, None),
        P(("seq", "pb")),
        P(),
        P(("seq", "pb"), None),
    )

    return jax.shard_map(
        per_device,
        mesh=mesh,
        in_specs=placed,
        out_specs=(P("seq", None), P(("seq", "pb"), None), P(("seq", "pb"), None), P()),
        check_vma=False,
    )
```
